1024 devices in a mesh: lat: 16 (over z_hi, x), lon: 64 (over y, z_lo, core).
Axes of the slice: x: 4, y: 4, z: 32 (z_hi: 4, z_lo: 8; z = z_hi * 8 + z_lo), core: 2. Of those that a mesh axis runs over, the one named last changes fastest.
Arguments:
- queries: bfloat16 [256, 512, 512], P('lat', 'lon'), may hold values from -48 to 48
- key_vectors: bfloat16 [256, 512, 512], P('lat', 'lon'), may hold values from -4 to 4
- value_vectors: bfloat16 [256, 512, 512], P('lat', 'lon'), may hold values from -6 to 6
- out_cotangent: bfloat16 [256, 512, 512], P('lat', 'lon'), may hold values from -6 to 6
- lat_start: int32 [256], P('lat'), may hold values from 0 to 243, as said below
- lon_start: int32 [512], P('lon'), may hold values from 0 to 511, as said below
- window_bias: float32 [8, 13, 13], replicated, may hold values from -4 to 4
Outputs:
- attention_out: bfloat16 [256, 512, 512], P('lat', 'lon')
- grad_queries: bfloat16 [256, 512, 512], P('lat', 'lon')
- grad_keys: bfloat16 [256, 512, 512], P('lat', 'lon')
- grad_values: bfloat16 [256, 512, 512], P('lat', 'lon')
- grad_window_bias: float32 [8, 13, 13], replicated
The draws below stay inside these ranges and needn't reach their ends.
Inputs may be any that keep to these rules, and one draw needn't show every extreme that they name: lat_start[i] differs from min(max(i - 6, 0), 243) by at most 2, and by exactly 2 and exactly -2 at some rows. lon_start[j] equals (j - 6 + e) mod 512 with e from -2 to 2; e = 2 and e = -2 both occur.
All inputs are finite; a program needn't handle non-finite values.
Results may differ from the reference program's by a relative error of at most 0.017.
Values may be sent and summed in bfloat16 or wider, within the bound.
No kernel may reach another device: no remote copies, remote signals or barrier semaphores. Data moves between devices by JAX's collectives and lax.ppermute only.
A program may use at most 64 MiB of HBM per device.

```python
import math
import jax
import jax.numpy as jnp
from jax import lax

D = 512
HEADS = 8
KW = 13
NLAT = 256
NLON = 512


def paired_fields(key):
    base = jax.random.fold_in(key, 11)
    query_key, vector_key = jax.random.split(base, 2)
    vectors = jnp.clip(jax.random.normal(vector_key, (NLAT, NLON, D), jnp.float32), -4.0, 4.0)
    queries = jnp.clip(jax.random.normal(query_key, (NLAT, NLON, D), jnp.float32), -4.0, 4.0)
    return (queries, vectors)


def draw_queries(key, part):
    return paired_fields(key)[0].astype(jnp.bfloat16)


def draw_key_vectors(key, part):
    return paired_fields(key)[1].astype(jnp.bfloat16)


def draw_lat_start(key, part):
    row_ids = jnp.arange(NLAT, dtype=jnp.int32)
    jitter = jax.random.randint(jax.random.fold_in(key, 3), (NLAT,), -2, 3, dtype=jnp.int32)
    jitter = jitter.at[0].set(0).at[NLAT - 1].set(0).at[NLAT // 2].set(2).at[NLAT // 2 + 1].set(-2)
    centre = jnp.clip(row_ids - 6, 0, NLAT - 13)
    return jnp.clip(centre + jitter, 0, NLAT - 13).astype(jnp.int32)


def draw_lon_start(key, part):
    col_ids = jnp.arange(NLON, dtype=jnp.int32)
    jitter = jax.random.randint(jax.random.fold_in(key, 5), (NLON,), -2, 3, dtype=jnp.int32)
    jitter = jitter.at[5].set(0).at[6].set(0).at[NLON // 2].set(2).at[NLON // 2 + 1].set(-2)
    return ((col_ids - 6 + jitter) % NLON).astype(jnp.int32)


def steps_of(rng, shape, cuts, low, high):
    level = 1.0
    for dim, blocks in cuts:
        draws = jax.random.uniform(jax.random.fold_in(jax.random.fold_in(rng, 6), dim), (blocks,), jnp.float32, low / len(cuts), high / len(cuts))
        level = level * jnp.repeat(jnp.exp(draws), shape[dim] // blocks).reshape((-1,) + (1,) * (len(shape) - 1 - dim))
    return level


def centred(key, extent, width, reach, shards=(), kind=jnp.bfloat16):
    array = width * jax.random.normal(key, extent, jnp.float32)
    if shards:
        array = array * steps_of(key, extent, shards, -0.22, 0.18)
    return jnp.clip(array, -reach, reach).astype(kind)


def setup_inputs(seed: int = 0) -> dict:
    arg_keys = jax.random.split(jax.random.key(seed), 8)
    return {
        "queries": draw_queries(jax.random.fold_in(arg_keys[7], 71), 0),
        "key_vectors": draw_key_vectors(jax.random.fold_in(arg_keys[7], 71), 0),
        "value_vectors": centred(arg_keys[2], (NLAT, NLON, D), 1.0, 6.0, ((0, 16), (1, 64))),
        "out_cotangent": centred(arg_keys[3], (NLAT, NLON, D), 1.0, 6.0, ((0, 16), (1, 64))),
        "lat_start": draw_lat_start(jax.random.fold_in(arg_keys[7], 71), 0),
        "lon_start": draw_lon_start(jax.random.fold_in(arg_keys[7], 71), 0),
        "window_bias": centred(arg_keys[6], (HEADS, KW, KW), 1.0, 4.0, (), jnp.float32),
    }


def tile_pass(query_tile, region, grad_tile, rel_rows, rel_cols, window_bias):
    head_count, window, _ = window_bias.shape
    model_width = query_tile.shape[-1]
    head_dim = model_width // head_count
    score_scale = head_dim ** -0.5
    query_heads = query_tile.reshape(64, head_count, head_dim).astype(jnp.float32)
    key_heads = region[..., :model_width].reshape(576, head_count, head_dim).astype(jnp.float32)
    value_heads = region[..., model_width:].reshape(576, head_count, head_dim).astype(jnp.float32)
    grad_heads = grad_tile.reshape(64, head_count, head_dim).astype(jnp.float32)
    offsets = jnp.arange(24, dtype=jnp.int32)
    places = jnp.arange(window, dtype=jnp.int32)
    row_hot = ((offsets[None, :, None] - rel_rows[:, None, None]) == places[None, None, :]).astype(jnp.float32)
    col_hot = ((offsets[None, :, None] - rel_cols[:, None, None]) == places[None, None, :]).astype(jnp.float32)
    half_bias = jnp.einsum('hpc,ikp->hikc', window_bias, row_hot)
    bias_tile = jnp.einsum('hikc,jlc->hijkl', half_bias, col_hot).reshape(head_count, 64, 576)
    inside = (jnp.sum(row_hot, -1)[:, None, :, None] * jnp.sum(col_hot, -1)[None, :, None, :]).reshape(64, 576) > 0.5
    scores = jnp.einsum('qhd,khd->hqk', query_heads, key_heads) * score_scale + bias_tile
    scores = jnp.where(inside[None], scores, -jnp.inf)
    row_peak = jnp.max(scores, axis=-1, keepdims=True)
    weights_raw = jnp.exp(scores - row_peak)
    attention = weights_raw / jnp.sum(weights_raw, axis=-1, keepdims=True)
    rounded_probs = attention.astype(jnp.bfloat16)
    output = jnp.einsum('hqk,khd->qhd', rounded_probs.astype(jnp.float32), value_heads)
    output = output.astype(jnp.bfloat16).reshape(8, 8, model_width)
    dprobs = jnp.einsum('qhd,khd->hqk', grad_heads, value_heads)
    dscore = attention * (dprobs - jnp.sum(attention * dprobs, axis=-1, keepdims=True))
    dscore_round = dscore.astype(jnp.bfloat16).astype(jnp.float32)
    grad_query_tile = (jnp.einsum('hqk,khd->qhd', dscore_round, key_heads) * score_scale)
    grad_query_tile = grad_query_tile.astype(jnp.bfloat16).reshape(8, 8, model_width)
    grad_keys = jnp.einsum('hqk,qhd->khd', dscore_round, query_heads) * score_scale
    grad_vals = jnp.einsum('hqk,qhd->khd', rounded_probs.astype(jnp.float32), grad_heads)
    grad_pairs = jnp.concatenate((grad_keys.reshape(24, 24, model_width), grad_vals.reshape(24, 24, model_width)), axis=-1)
    half_table = jnp.einsum('hijkl,jlc->hikc', dscore.reshape(head_count, 8, 8, 24, 24), col_hot)
    grad_table = jnp.einsum('hikc,ikp->hpc', half_table, row_hot)
    return output, grad_query_tile, grad_pairs, grad_table


def reference(queries, key_vectors, value_vectors, out_cotangent, lat_start, lon_start, window_bias):
    lat_rows, lon_cols, model_width = queries.shape
    band_count = lat_rows // 8
    tile_count = lon_cols // 8
    group_size = math.gcd(tile_count, 16)
    offsets = jnp.arange(24, dtype=jnp.int32)
    tile_firsts = jnp.arange(tile_count, dtype=jnp.int32) * 8 - 8
    col_index = (tile_firsts[:, None] + offsets[None, :]) % lon_cols
    rel_cols_all = (lon_start.reshape(tile_count, 8) - tile_firsts[:, None]) % lon_cols

    def to_tiles(band):
        return band.reshape(8, tile_count, 8, model_width).transpose(1, 0, 2, 3)

    def advance(pending, band):
        pend_low, pend_high, table_sum = pending
        row_index = band * 8 - 8 + offsets
        inside_grid = (row_index >= 0) & (row_index < lat_rows)
        clipped = jnp.clip(row_index, 0, lat_rows - 1).astype(jnp.int32)
        pair_rows = jnp.concatenate((jnp.take(key_vectors, clipped, axis=0), jnp.take(value_vectors, clipped, axis=0)), axis=-1)
        pair_rows = jnp.where(inside_grid[:, None, None], pair_rows, jnp.zeros_like(pair_rows))
        regions = jnp.take(pair_rows, col_index, axis=1).transpose(1, 0, 2, 3)
        query_band = to_tiles(lax.dynamic_slice_in_dim(queries, band * 8, 8, 0))
        grad_band = to_tiles(lax.dynamic_slice_in_dim(out_cotangent, band * 8, 8, 0))
        rel_rows = lax.dynamic_slice_in_dim(lat_start, band * 8, 8, 0) - (band * 8 - 8)

        def run_group(members):
            return jax.vmap(lambda qt, rg, gt, rc: tile_pass(qt, rg, gt, rel_rows, rc, window_bias))(*members)

        shaped = tuple(item.reshape((tile_count // group_size, group_size) + item.shape[1:]) for item in (query_band, regions, grad_band, rel_cols_all))
        results = lax.map(run_group, shaped)
        results = tuple(item.reshape((tile_count,) + item.shape[2:]) for item in results)
        tile_out, tile_grad, tile_pairs, tile_table = results
        band_out = tile_out.transpose(1, 0, 2, 3).reshape(8, lon_cols, model_width)
        band_grad = tile_grad.transpose(1, 0, 2, 3).reshape(8, lon_cols, model_width)
        blocks = tile_pairs.reshape(tile_count, 24, 3, 8, 2 * model_width)
        summed = jnp.roll(blocks[:, :, 0], -1, axis=0) + blocks[:, :, 1] + jnp.roll(blocks[:, :, 2], 1, axis=0)
        band_pairs = summed.transpose(1, 0, 2, 3).reshape(24, lon_cols, 2 * model_width)
        finished = pend_low + band_pairs[:8]
        pending = (pend_high + band_pairs[8:16], band_pairs[16:], table_sum + jnp.sum(tile_table, axis=0))
        return pending, (band_out, band_grad, finished.astype(jnp.bfloat16))

    empty = jnp.zeros((8, lon_cols, 2 * model_width), jnp.float32)
    start_state = (empty, empty, jnp.zeros(window_bias.shape, jnp.float32))
    final_state, stacked = lax.scan(advance, start_state, jnp.arange(band_count, dtype=jnp.int32))
    last_low, last_high, table_sum = final_state
    outs_all, grads_all, pairs_all = stacked
    attention_out = outs_all.reshape(lat_rows, lon_cols, model_width)
    grad_queries = grads_all.reshape(lat_rows, lon_cols, model_width)
    pair_grads = jnp.concatenate((pairs_all[1:].reshape(-1, lon_cols, 2 * model_width), last_low.astype(jnp.bfloat16)), axis=0)
    grad_keys = pair_grads[..., :model_width]
    grad_values = pair_grads[..., model_width:]
    return (attention_out, grad_queries, grad_keys, grad_values, table_sum)
```

```python
import jax
import jax.numpy as jnp
from jax import lax
from jax.sharding import PartitionSpec as P


def padded_2(value, sides, width, wrap):
    for axis, dim in sides:
        size, length = (lax.axis_size(axis), value.shape[dim])
        up = [(i, (i + 1) % size) for i in range(size if wrap else size - 1)]
        down = [(j, i) for i, j in up]
        last = lax.slice_in_dim(value, length - width, length, axis=dim)
        leading = lax.slice_in_dim(value, 0, width, axis=dim)
        before = lax.ppermute(last, axis, up)
        after = lax.ppermute(leading, axis, down)
        value = jnp.concatenate([before, value, after], axis=dim)
    return value


def place_tables(row_hot, col_hot):
    row_merged = jnp.repeat(row_hot.transpose(1, 2, 0), 24, axis=-1)
    col_merged = jnp.tile(col_hot.transpose(1, 2, 0), (1, 1, 24))
    return (row_merged, col_merged)


def place_bias(window_bias, row_merged, col_hot):
    col_part = jnp.einsum("hpc,ljc->hpjl", window_bias, col_hot)
    col_spread = jnp.tile(col_part, (1, 1, 1, 24))
    bias = jnp.sum(row_merged[None, :, :, None, :] * col_spread[:, None, :, :, :], axis=2)
    return bias.reshape(window_bias.shape[0], 64, 576)


def place_table(dscore, row_merged, col_merged):
    head_count = dscore.shape[0]
    shaped = dscore.reshape(head_count, 8, 8, 576)
    by_row = jnp.sum(shaped[:, :, None, :, :] * row_merged[None, :, :, None, :], axis=1)
    return jnp.einsum("hpjk,jck->hpc", by_row, col_merged)


def inside_mask(row_merged, col_merged):
    row_in = jnp.sum(row_merged, axis=1)
    col_in = jnp.sum(col_merged, axis=1)
    return (row_in[:, None, :] * col_in[None, :, :]).reshape(64, 576) > 0.5


def tile_pass(query_tile, region, grad_tile, rel_rows, rel_cols, window_bias):
    head_count, window, _ = window_bias.shape
    model_width = query_tile.shape[-1]
    head_dim = model_width // head_count
    score_scale = head_dim ** (-0.5)
    query_heads = query_tile.reshape(64, head_count, head_dim)
    key_heads = region[..., :model_width].reshape(576, head_count, head_dim)
    value_heads = region[..., model_width:].reshape(576, head_count, head_dim)
    grad_heads = grad_tile.reshape(64, head_count, head_dim)
    offsets = jnp.arange(24, dtype=jnp.int32)
    places = jnp.arange(window, dtype=jnp.int32)
    row_hot = (offsets[:, None, None] - rel_rows[None, :, None] == places[None, None, :]).astype(
        jnp.float32
    )
    col_hot = (offsets[:, None, None] - rel_cols[None, :, None] == places[None, None, :]).astype(
        jnp.float32
    )
    row_merged, col_merged = place_tables(row_hot, col_hot)
    bias_tile = place_bias(window_bias, row_merged, col_hot)
    inside = inside_mask(row_merged, col_merged)
    scores = (
        jnp.einsum("qhd,khd->hqk", query_heads, key_heads, preferred_element_type=jnp.float32)
        * score_scale
        + bias_tile
    )
    scores = jnp.where(inside[None], scores, -jnp.inf)
    row_peak = jnp.max(scores, axis=-1, keepdims=True)
    weights_raw = jnp.exp(scores - row_peak)
    row_total = jnp.sum(weights_raw, axis=-1, keepdims=True)
    attention = weights_raw / row_total
    rounded_probs = attention.astype(jnp.bfloat16)
    output = jnp.einsum(
        "hqk,khd->qhd", rounded_probs, value_heads, preferred_element_type=jnp.float32
    )
    output = output.astype(jnp.bfloat16).reshape(8, 8, model_width)
    dprobs = jnp.einsum("qhd,khd->hqk", grad_heads, value_heads, preferred_element_type=jnp.float32)
    correction = jnp.sum(attention * dprobs, axis=-1, keepdims=True)
    dscore = attention * (dprobs - correction)
    dscore_round = dscore.astype(jnp.bfloat16)
    grad_query_tile = (
        jnp.einsum("hqk,khd->qhd", dscore_round, key_heads, preferred_element_type=jnp.float32)
        * score_scale
    )
    grad_query_tile = grad_query_tile.astype(jnp.bfloat16).reshape(8, 8, model_width)
    grad_table = place_table(dscore, row_merged, col_merged)
    log_total = (row_peak + jnp.log(row_total))[..., 0]
    statistics = jnp.concatenate((log_total.T, correction[..., 0].T), axis=-1).reshape(
        8, 8, 2 * head_count
    )
    grad_keys = (
        jnp.einsum("hqk,qhd->khd", dscore_round, query_heads, preferred_element_type=jnp.float32)
        * score_scale
    )
    grad_vals = jnp.einsum(
        "hqk,qhd->khd", rounded_probs, grad_heads, preferred_element_type=jnp.float32
    )
    grad_pairs = jnp.concatenate(
        (grad_keys.reshape(24, 24, model_width), grad_vals.reshape(24, 24, model_width)), axis=-1
    )
    return (output, grad_query_tile, grad_pairs, grad_table, statistics)


def rims_of(array, along):
    if along == 0:
        return jnp.concatenate((array[:8], array[-8:]), axis=0)
    return jnp.concatenate((array[:, :8], array[:, -8:]), axis=1)


def settle(array, arrived, along):
    if along == 0:
        inner = array[8:-8]
        inner = inner.at[:8].add(arrived[:8])
        return inner.at[-8:].add(arrived[-8:])
    inner = array[:, 8:-8]
    inner = inner.at[:, :8].add(arrived[:, :8])
    return inner.at[:, -8:].add(arrived[:, -8:])


def exchange_sum(value, axis, flip):
    size = lax.axis_size(axis)
    pairs = [(i, i ^ flip) for i in range(size)]
    return value + lax.ppermute(value, axis, pairs)


def all_sum(value):
    for axis, flips in (("lon", (1, 2, 4, 8, 16, 48)), ("lat", (1, 3, 4, 12))):
        for flip in flips:
            value = exchange_sum(value, axis, flip)
    return value


def per_device(
    queries, key_vectors, value_vectors, out_cotangent, lat_start, lon_start, window_bias
):
    height, breadth, model_width = queries.shape
    lon_total = breadth * lax.axis_size("lon")
    first_row = lax.axis_index("lat") * height
    first_col = lax.axis_index("lon") * breadth
    stacked = jnp.concatenate((key_vectors, value_vectors), axis=-1)
    widened = padded_2(stacked, (("lon", 1),), 8, True)
    padded = padded_2(widened, (("lat", 0),), 8, False)
    across = breadth // 8
    tile_total = height // 8 * across

    def tile_inputs(tile_index):
        tile_row = tile_index // across * 8
        tile_col = tile_index % across * 8
        region = lax.dynamic_slice(padded, (tile_row, tile_col, 0), (24, 24, 2 * model_width))
        query_tile = lax.dynamic_slice(queries, (tile_row, tile_col, 0), (8, 8, model_width))
        grad_tile = lax.dynamic_slice(out_cotangent, (tile_row, tile_col, 0), (8, 8, model_width))
        rel_rows = lax.dynamic_slice_in_dim(lat_start, tile_row, 8, 0) - (first_row + tile_row - 8)
        rel_cols = (lon_start - (first_col + tile_col - 8)) % lon_total
        return (tile_row, tile_col, query_tile, region, grad_tile, rel_rows, rel_cols)

    def visit(tile_index, state):
        accum, output, grad_query, grad_table = state
        tile_row, tile_col, query_tile, region, grad_tile, rel_rows, rel_cols = tile_inputs(
            tile_index
        )
        tile_out, tile_grad, tile_pairs, tile_table, unused = tile_pass(
            query_tile, region, grad_tile, rel_rows, rel_cols, window_bias
        )
        current = lax.dynamic_slice(accum, (tile_row, tile_col, 0), (24, 24, 2 * model_width))
        accum = lax.dynamic_update_slice(accum, current + tile_pairs, (tile_row, tile_col, 0))
        output = lax.dynamic_update_slice(output, tile_out, (tile_row, tile_col, 0))
        grad_query = lax.dynamic_update_slice(grad_query, tile_grad, (tile_row, tile_col, 0))
        return (accum, output, grad_query, grad_table + tile_table)

    start_state = (
        jnp.zeros((height + 16, breadth + 16, 2 * model_width), jnp.float32),
        jnp.zeros(queries.shape, jnp.bfloat16),
        jnp.zeros(queries.shape, jnp.bfloat16),
        jnp.zeros(window_bias.shape, jnp.float32),
    )
    accum, attention_out, grad_queries, grad_table = lax.fori_loop(
        0, tile_total, visit, start_state
    )
    arrived = padded_2(rims_of(accum, 0).astype(jnp.bfloat16), (("lat", 0),), 8, False).astype(
        jnp.float32
    )
    folded = settle(accum, arrived, 0)
    arrived_cols = padded_2(rims_of(folded, 1).astype(jnp.bfloat16), (("lon", 1),), 8, True).astype(
        jnp.float32
    )
    totals = settle(folded, arrived_cols, 1)
    grad_keys = totals[..., :model_width].astype(jnp.bfloat16)
    grad_values = totals[..., model_width:].astype(jnp.bfloat16)
    grad_window_bias = all_sum(grad_table)
    return (attention_out, grad_queries, grad_keys, grad_values, grad_window_bias)


def solution(mesh):
    return jax.shard_map(
        per_device,
        mesh=mesh,
        in_specs=(
            P("lat", "lon", None),
            P("lat", "lon", None),
            P("lat", "lon", None),
            P("lat", "lon", None),
            P("lat"),
            P("lon"),
            P(),
        ),
        out_specs=(
            P("lat", "lon", None),
            P("lat", "lon", None),
            P("lat", "lon", None),
            P("lat", "lon", None),
            P(),
        ),
        check_vma=False,
    )
```

```python
import jax
import jax.numpy as jnp
from jax import lax
from jax.sharding import PartitionSpec as P


def padded_2(value, sides, width, wrap):
    for axis, dim in sides:
        size, length = (lax.axis_size(axis), value.shape[dim])
        up = [(i, (i + 1) % size) for i in range(size if wrap else size - 1)]
        down = [(j, i) for i, j in up]
        last = lax.slice_in_dim(value, length - width, length, axis=dim)
        leading = lax.slice_in_dim(value, 0, width, axis=dim)
        before = lax.ppermute(last, axis, up)
        after = lax.ppermute(leading, axis, down)
        value = jnp.concatenate([before, value, after], axis=dim)
    return value


def place_tables(row_hot, col_hot):
    row_merged = jnp.repeat(row_hot.transpose(1, 2, 0), 24, axis=-1)
    col_merged = jnp.tile(col_hot.transpose(1, 2, 0), (1, 1, 24))
    return (row_merged, col_merged)


def place_bias(window_bias, row_merged, col_hot):
    col_part = jnp.einsum("hpc,ljc->hpjl", window_bias, col_hot)
    col_spread = jnp.tile(col_part, (1, 1, 1, 24))
    bias = jnp.sum(row_merged[None, :, :, None, :] * col_spread[:, None, :, :, :], axis=2)
    return bias.reshape(window_bias.shape[0], 64, 576)


def place_table(dscore, row_merged, col_merged):
    head_count = dscore.shape[0]
    shaped = dscore.reshape(head_count, 8, 8, 576)
    by_row = jnp.sum(shaped[:, :, None, :, :] * row_merged[None, :, :, None, :], axis=1)
    return jnp.einsum("hpjk,jck->hpc", by_row, col_merged)


def inside_mask(row_merged, col_merged):
    row_in = jnp.sum(row_merged, axis=1)
    col_in = jnp.sum(col_merged, axis=1)
    return (row_in[:, None, :] * col_in[None, :, :]).reshape(64, 576) > 0.5


def tile_pass(query_tile, region, grad_tile, rel_rows, rel_cols, window_bias):
    head_count, window, _ = window_bias.shape
    model_width = query_tile.shape[-1]
    head_dim = model_width // head_count
    score_scale = head_dim ** (-0.5)
    query_heads = query_tile.reshape(64, head_count, head_dim)
    key_heads = region[..., :model_width].reshape(576, head_count, head_dim)
    value_heads = region[..., model_width:].reshape(576, head_count, head_dim)
    grad_heads = grad_tile.reshape(64, head_count, head_dim)
    offsets = jnp.arange(24, dtype=jnp.int32)
    places = jnp.arange(window, dtype=jnp.int32)
    row_hot = (offsets[:, None, None] - rel_rows[None, :, None] == places[None, None, :]).astype(
        jnp.float32
    )
    col_hot = (offsets[:, None, None] - rel_cols[None, :, None] == places[None, None, :]).astype(
        jnp.float32
    )
    row_merged, col_merged = place_tables(row_hot, col_hot)
    bias_tile = place_bias(window_bias, row_merged, col_hot)
    inside = inside_mask(row_merged, col_merged)
    scores = (
        jnp.einsum("qhd,khd->hqk", query_heads, key_heads, preferred_element_type=jnp.float32)
        * score_scale
        + bias_tile
    )
    scores = jnp.where(inside[None], scores, -jnp.inf)
    row_peak = jnp.max(scores, axis=-1, keepdims=True)
    weights_raw = jnp.exp(scores - row_peak)
    row_total = jnp.sum(weights_raw, axis=-1, keepdims=True)
    attention = weights_raw / row_total
    rounded_probs = attention.astype(jnp.bfloat16)
    output = jnp.einsum(
        "hqk,khd->qhd", rounded_probs, value_heads, preferred_element_type=jnp.float32
    )
    output = output.astype(jnp.bfloat16).reshape(8, 8, model_width)
    dprobs = jnp.einsum("qhd,khd->hqk", grad_heads, value_heads, preferred_element_type=jnp.float32)
    correction = jnp.sum(attention * dprobs, axis=-1, keepdims=True)
    dscore = attention * (dprobs - correction)
    dscore_round = dscore.astype(jnp.bfloat16)
    grad_query_tile = (
        jnp.einsum("hqk,khd->qhd", dscore_round, key_heads, preferred_element_type=jnp.float32)
        * score_scale
    )
    grad_query_tile = grad_query_tile.astype(jnp.bfloat16).reshape(8, 8, model_width)
    grad_table = place_table(dscore, row_merged, col_merged)
    log_total = (row_peak + jnp.log(row_total))[..., 0]
    statistics = jnp.concatenate((log_total.T, correction[..., 0].T), axis=-1).reshape(
        8, 8, 2 * head_count
    )
    grad_keys = (
        jnp.einsum("hqk,qhd->khd", dscore_round, query_heads, preferred_element_type=jnp.float32)
        * score_scale
    )
    grad_vals = jnp.einsum(
        "hqk,qhd->khd", rounded_probs, grad_heads, preferred_element_type=jnp.float32
    )
    grad_pairs = jnp.concatenate(
        (grad_keys.reshape(24, 24, model_width), grad_vals.reshape(24, 24, model_width)), axis=-1
    )
    return (output, grad_query_tile, grad_pairs, grad_table, statistics)


def rims_of(array, along):
    if along == 0:
        return jnp.concatenate((array[:8], array[-8:]), axis=0)
    return jnp.concatenate((array[:, :8], array[:, -8:]), axis=1)


def settle(array, arrived, along):
    if along == 0:
        inner = array[8:-8]
        inner = inner.at[:8].add(arrived[:8])
        return inner.at[-8:].add(arrived[-8:])
    inner = array[:, 8:-8]
    inner = inner.at[:, :8].add(arrived[:, :8])
    return inner.at[:, -8:].add(arrived[:, -8:])


def exchange_sum(value, axis, flip):
    size = lax.axis_size(axis)
    pairs = [(i, i ^ flip) for i in range(size)]
    return value + lax.ppermute(value, axis, pairs)


def all_sum(value):
    for axis, flips in (("lon", (1, 2, 4, 8, 16, 48)), ("lat", (1, 3, 4, 12))):
        for flip in flips:
            value = exchange_sum(value, axis, flip)
    return value


def per_device(
    queries, key_vectors, value_vectors, out_cotangent, lat_start, lon_start, window_bias
):
    height, breadth, model_width = queries.shape
    lon_total = breadth * lax.axis_size("lon")
    first_row = lax.axis_index("lat") * height
    first_col = lax.axis_index("lon") * breadth
    stacked = jnp.concatenate((key_vectors, value_vectors), axis=-1)
    tall = padded_2(stacked, (("lat", 0),), 8, False)
    padded = padded_2(tall, (("lon", 1),), 8, True)
    across = breadth // 8
    tile_total = height // 8 * across

    def tile_inputs(tile_index):
        tile_row = tile_index // across * 8
        tile_col = tile_index % across * 8
        region = lax.dynamic_slice(padded, (tile_row, tile_col, 0), (24, 24, 2 * model_width))
        query_tile = lax.dynamic_slice(queries, (tile_row, tile_col, 0), (8, 8, model_width))
        grad_tile = lax.dynamic_slice(out_cotangent, (tile_row, tile_col, 0), (8, 8, model_width))
        rel_rows = lax.dynamic_slice_in_dim(lat_start, tile_row, 8, 0) - (first_row + tile_row - 8)
        rel_cols = (lon_start - (first_col + tile_col - 8)) % lon_total
        return (tile_row, tile_col, query_tile, region, grad_tile, rel_rows, rel_cols)

    def visit(tile_index, state):
        accum, output, grad_query, grad_table = state
        tile_row, tile_col, query_tile, region, grad_tile, rel_rows, rel_cols = tile_inputs(
            tile_index
        )
        tile_out, tile_grad, tile_pairs, tile_table, unused = tile_pass(
            query_tile, region, grad_tile, rel_rows, rel_cols, window_bias
        )
        current = lax.dynamic_slice(accum, (tile_row, tile_col, 0), (24, 24, 2 * model_width))
        accum = lax.dynamic_update_slice(accum, current + tile_pairs, (tile_row, tile_col, 0))
        output = lax.dynamic_update_slice(output, tile_out, (tile_row, tile_col, 0))
        grad_query = lax.dynamic_update_slice(grad_query, tile_grad, (tile_row, tile_col, 0))
        return (accum, output, grad_query, grad_table + tile_table)

    start_state = (
        jnp.zeros((height + 16, breadth + 16, 2 * model_width), jnp.float32),
        jnp.zeros(queries.shape, jnp.bfloat16),
        jnp.zeros(queries.shape, jnp.bfloat16),
        jnp.zeros(window_bias.shape, jnp.float32),
    )
    accum, attention_out, grad_queries, grad_table = lax.fori_loop(
        0, tile_total, visit, start_state
    )
    arrived_cols = padded_2(rims_of(accum, 1).astype(jnp.bfloat16), (("lon", 1),), 8, True).astype(
        jnp.float32
    )
    folded = settle(accum, arrived_cols, 1)
    arrived = padded_2(rims_of(folded, 0).astype(jnp.bfloat16), (("lat", 0),), 8, False).astype(
        jnp.float32
    )
    totals = settle(folded, arrived, 0)
    grad_keys = totals[..., :model_width].astype(jnp.bfloat16)
    grad_values = totals[..., model_width:].astype(jnp.bfloat16)
    grad_window_bias = all_sum(grad_table)
    return (attention_out, grad_queries, grad_keys, grad_values, grad_window_bias)


def solution(mesh):
    return jax.shard_map(
        per_device,
        mesh=mesh,
        in_specs=(
            P("lat", "lon", None),
            P("lat", "lon", None),
            P("lat", "lon", None),
            P("lat", "lon", None),
            P("lat"),
            P("lon"),
            P(),
        ),
        out_specs=(
            P("lat", "lon", None),
            P("lat", "lon", None),
            P("lat", "lon", None),
            P("lat", "lon", None),
            P(),
        ),
        check_vma=False,
    )
```

```python
import jax
import jax.numpy as jnp
from jax import lax
from jax.sharding import PartitionSpec as P


def padded_2(value, sides, width, wrap):
    for axis, dim in sides:
        size, length = (lax.axis_size(axis), value.shape[dim])
        up = [(i, (i + 1) % size) for i in range(size if wrap else size - 1)]
        down = [(j, i) for i, j in up]
        last = lax.slice_in_dim(value, length - width, length, axis=dim)
        leading = lax.slice_in_dim(value, 0, width, axis=dim)
        before = lax.ppermute(last, axis, up)
        after = lax.ppermute(leading, axis, down)
        value = jnp.concatenate([before, value, after], axis=dim)
    return value


def rims_of(array, along):
    if along == 0:
        return jnp.concatenate((array[:8], array[-8:]), axis=0)
    return jnp.concatenate((array[:, :8], array[:, -8:]), axis=1)


def settle(array, arrived, along):
    if along == 0:
        inner = array[8:-8]
        inner = inner.at[:8].add(arrived[:8])
        return inner.at[-8:].add(arrived[-8:])
    inner = array[:, 8:-8]
    inner = inner.at[:, :8].add(arrived[:, :8])
    return inner.at[:, -8:].add(arrived[:, -8:])


def exchange_sum(value, axis, flip):
    size = lax.axis_size(axis)
    pairs = [(i, i ^ flip) for i in range(size)]
    return value + lax.ppermute(value, axis, pairs)


def all_sum(value):
    for axis, flips in (("lon", (1, 2, 4, 8, 16, 48)), ("lat", (1, 3, 4, 12))):
        for flip in flips:
            value = exchange_sum(value, axis, flip)
    return value


def per_device(
    queries, key_vectors, value_vectors, out_cotangent, lat_start, lon_start, window_bias
):
    height, breadth, model_width = queries.shape
    head_count, window, _ = window_bias.shape
    head_dim = model_width // head_count
    score_scale = head_dim ** (-0.5)
    lon_total = breadth * lax.axis_size("lon")
    first_row = lax.axis_index("lat") * height
    first_col = lax.axis_index("lon") * breadth
    stacked = jnp.concatenate((key_vectors, value_vectors), axis=-1)
    tall = padded_2(stacked, (("lat", 0),), 8, False)
    padded = padded_2(tall, (("lon", 1),), 8, True)
    rows, cols = height + 16, breadth + 16
    cells, keys = height * breadth, rows * cols
    exact = lax.Precision.HIGHEST

    rel_rows = lat_start - (first_row - 8)
    rel_cols = (lon_start - (first_col - 8)) % lon_total
    places = jnp.arange(window, dtype=jnp.int32)
    row_hot = (
        jnp.arange(rows, dtype=jnp.int32)[None, :, None] - rel_rows[:, None, None] == places
    ).astype(jnp.float32)
    col_hot = (
        jnp.arange(cols, dtype=jnp.int32)[None, :, None] - rel_cols[:, None, None] == places
    ).astype(jnp.float32)
    half_bias = jnp.einsum("hab,ira->hirb", window_bias, row_hot, precision=exact)
    bias = jnp.einsum("hirb,jcb->hijrc", half_bias, col_hot, precision=exact)
    bias = bias.reshape(head_count, cells, keys)
    inside = jnp.sum(row_hot, -1)[:, None, :, None] * jnp.sum(col_hot, -1)[None, :, None, :]
    inside = inside.reshape(cells, keys) > 0.5

    query_heads = queries.reshape(cells, head_count, head_dim)
    key_heads = padded[..., :model_width].reshape(keys, head_count, head_dim)
    value_heads = padded[..., model_width:].reshape(keys, head_count, head_dim)
    grad_heads = out_cotangent.reshape(cells, head_count, head_dim)
    scores = (
        jnp.einsum("qhd,khd->hqk", query_heads, key_heads, preferred_element_type=jnp.float32)
        * score_scale
        + bias
    )
    scores = jnp.where(inside[None], scores, -jnp.inf)
    row_peak = jnp.max(scores, axis=-1, keepdims=True)
    weights_raw = jnp.exp(scores - row_peak)
    row_total = jnp.sum(weights_raw, axis=-1, keepdims=True)
    attention = weights_raw / row_total
    rounded_probs = attention.astype(jnp.bfloat16)
    output = jnp.einsum(
        "hqk,khd->qhd", rounded_probs, value_heads, preferred_element_type=jnp.float32
    )
    attention_out = output.astype(jnp.bfloat16).reshape(height, breadth, model_width)
    dprobs = jnp.einsum("qhd,khd->hqk", grad_heads, value_heads, preferred_element_type=jnp.float32)
    correction = jnp.sum(attention * dprobs, axis=-1, keepdims=True)
    dscore = attention * (dprobs - correction)
    dscore_round = dscore.astype(jnp.bfloat16)
    grad_query = (
        jnp.einsum("hqk,khd->qhd", dscore_round, key_heads, preferred_element_type=jnp.float32)
        * score_scale
    )
    grad_queries = grad_query.astype(jnp.bfloat16).reshape(height, breadth, model_width)
    by_col = jnp.einsum(
        "hijrc,jcb->hirb",
        dscore.reshape(head_count, height, breadth, rows, cols),
        col_hot,
        precision=exact,
    )
    grad_table = jnp.einsum("hirb,ira->hab", by_col, row_hot, precision=exact)
    grad_keys = (
        jnp.einsum("hqk,qhd->khd", dscore_round, query_heads, preferred_element_type=jnp.float32)
        * score_scale
    )
    grad_vals = jnp.einsum(
        "hqk,qhd->khd", rounded_probs, grad_heads, preferred_element_type=jnp.float32
    )
    accum = jnp.concatenate(
        (grad_keys.reshape(rows, cols, model_width), grad_vals.reshape(rows, cols, model_width)),
        axis=-1,
    )
    arrived_cols = padded_2(rims_of(accum, 1).astype(jnp.bfloat16), (("lon", 1),), 8, True).astype(
        jnp.float32
    )
    folded = settle(accum, arrived_cols, 1)
    arrived = padded_2(rims_of(folded, 0).astype(jnp.bfloat16), (("lat", 0),), 8, False).astype(
        jnp.float32
    )
    totals = settle(folded, arrived, 0)
    grad_keys = totals[..., :model_width].astype(jnp.bfloat16)
    grad_values = totals[..., model_width:].astype(jnp.bfloat16)
    grad_window_bias = all_sum(grad_table)
    return (attention_out, grad_queries, grad_keys, grad_values, grad_window_bias)


def solution(mesh):
    return jax.shard_map(
        per_device,
        mesh=mesh,
        in_specs=(
            P("lat", "lon", None),
            P("lat", "lon", None),
            P("lat", "lon", None),
            P("lat", "lon", None),
            P("lat"),
            P("lon"),
            P(),
        ),
        out_specs=(
            P("lat", "lon", None),
            P("lat", "lon", None),
            P("lat", "lon", None),
            P("lat", "lon", None),
            P(),
        ),
        check_vma=False,
    )
```

```python
import jax
import jax.numpy as jnp
from jax import lax
from jax.sharding import PartitionSpec as P


def padded_2(value, sides, width, wrap):
    for axis, dim in sides:
        size, length = (lax.axis_size(axis), value.shape[dim])
        up = [(i, (i + 1) % size) for i in range(size if wrap else size - 1)]
        down = [(j, i) for i, j in up]
        last = lax.slice_in_dim(value, length - width, length, axis=dim)
        leading = lax.slice_in_dim(value, 0, width, axis=dim)
        before = lax.ppermute(last, axis, up)
        after = lax.ppermute(leading, axis, down)
        value = jnp.concatenate([before, value, after], axis=dim)
    return value


def rims_of(array, along):
    if along == 0:
        return jnp.concatenate((array[:8], array[-8:]), axis=0)
    return jnp.concatenate((array[:, :8], array[:, -8:]), axis=1)


def settle(array, arrived, along):
    if along == 0:
        inner = array[8:-8]
        inner = inner.at[:8].add(arrived[:8])
        return inner.at[-8:].add(arrived[-8:])
    inner = array[:, 8:-8]
    inner = inner.at[:, :8].add(arrived[:, :8])
    return inner.at[:, -8:].add(arrived[:, -8:])


def exchange_sum(value, axis, flip):
    size = lax.axis_size(axis)
    pairs = [(i, i ^ flip) for i in range(size)]
    return value + lax.ppermute(value, axis, pairs)


def all_sum(value):
    for axis, flips in (("lon", (1, 2, 4, 8, 16, 48)), ("lat", (1, 3, 4, 12))):
        for flip in flips:
            value = exchange_sum(value, axis, flip)
    return value


def per_device(
    queries, key_vectors, value_vectors, out_cotangent, lat_start, lon_start, window_bias
):
    height, breadth, model_width = queries.shape
    head_count, window, _ = window_bias.shape
    head_dim = model_width // head_count
    score_scale = head_dim ** (-0.5)
    lon_total = breadth * lax.axis_size("lon")
    first_row = lax.axis_index("lat") * height
    first_col = lax.axis_index("lon") * breadth
    stacked = jnp.concatenate((key_vectors, value_vectors), axis=-1)
    tall = padded_2(stacked, (("lat", 0),), 8, False)
    padded = padded_2(tall, (("lon", 1),), 8, True)
    rows, cols = height + 16, breadth + 16
    cells, keys = height * breadth, rows * cols
    exact = lax.Precision.HIGHEST

    rel_rows = lat_start - (first_row - 8)
    rel_cols = (lon_start - (first_col - 8)) % lon_total
    places = jnp.arange(window, dtype=jnp.int32)
    key_index = jnp.arange(keys, dtype=jnp.int32)
    row_off = (key_index // cols)[None, :] - rel_rows[:, None]
    col_off = (key_index % cols)[None, :] - rel_cols[:, None]
    row_hot = (row_off[:, None, :] == places[None, :, None]).astype(jnp.float32)
    col_hot = (col_off[:, None, :] == places[None, :, None]).astype(jnp.float32)
    half_bias = jnp.sum(window_bias[:, None, :, :, None] * row_hot[None, :, :, None, :], axis=2)
    bias = jnp.sum(half_bias[:, :, None, :, :] * col_hot[None, None, :, :, :], axis=3)
    bias = bias.reshape(head_count, cells, keys)
    row_in = (row_off >= 0) & (row_off < window)
    col_in = (col_off >= 0) & (col_off < window)
    inside = (row_in[:, None, :] & col_in[None, :, :]).reshape(cells, keys)

    query_heads = queries.reshape(cells, head_count, head_dim)
    key_heads = padded[..., :model_width].reshape(keys, head_count, head_dim)
    value_heads = padded[..., model_width:].reshape(keys, head_count, head_dim)
    grad_heads = out_cotangent.reshape(cells, head_count, head_dim)
    scores = (
        jnp.einsum("qhd,khd->hqk", query_heads, key_heads, preferred_element_type=jnp.float32)
        * score_scale
        + bias
    )
    scores = jnp.where(inside[None], scores, -jnp.inf)
    row_peak = jnp.max(scores, axis=-1, keepdims=True)
    weights_raw = jnp.exp(scores - row_peak)
    row_total = jnp.sum(weights_raw, axis=-1, keepdims=True)
    attention = weights_raw / row_total
    rounded_probs = attention.astype(jnp.bfloat16)
    output = jnp.einsum(
        "hqk,khd->qhd", rounded_probs, value_heads, preferred_element_type=jnp.float32
    )
    attention_out = output.astype(jnp.bfloat16).reshape(height, breadth, model_width)
    dprobs = jnp.einsum("qhd,khd->hqk", grad_heads, value_heads, preferred_element_type=jnp.float32)
    correction = jnp.sum(attention * dprobs, axis=-1, keepdims=True)
    dscore = attention * (dprobs - correction)
    dscore_round = dscore.astype(jnp.bfloat16)
    grad_query = (
        jnp.einsum("hqk,khd->qhd", dscore_round, key_heads, preferred_element_type=jnp.float32)
        * score_scale
    )
    grad_queries = grad_query.astype(jnp.bfloat16).reshape(height, breadth, model_width)
    grad_cells = dscore.reshape(head_count, height, breadth, keys)
    by_col = jnp.sum(grad_cells[:, :, :, None, :] * col_hot[None, None, :, :, :], axis=2)
    grad_table = jnp.einsum("hibk,iak->hab", by_col, row_hot, precision=exact)
    grad_keys = (
        jnp.einsum("hqk,qhd->khd", dscore_round, query_heads, preferred_element_type=jnp.float32)
        * score_scale
    )
    grad_vals = jnp.einsum(
        "hqk,qhd->khd", rounded_probs, grad_heads, preferred_element_type=jnp.float32
    )
    accum = jnp.concatenate(
        (grad_keys.reshape(rows, cols, model_width), grad_vals.reshape(rows, cols, model_width)),
        axis=-1,
    )
    arrived_cols = padded_2(rims_of(accum, 1).astype(jnp.bfloat16), (("lon", 1),), 8, True).astype(
        jnp.float32
    )
    folded = settle(accum, arrived_cols, 1)
    arrived = padded_2(rims_of(folded, 0).astype(jnp.bfloat16), (("lat", 0),), 8, False).astype(
        jnp.float32
    )
    totals = settle(folded, arrived, 0)
    grad_keys = totals[..., :model_width].astype(jnp.bfloat16)
    grad_values = totals[..., model_width:].astype(jnp.bfloat16)
    grad_window_bias = all_sum(grad_table)
    return (attention_out, grad_queries, grad_keys, grad_values, grad_window_bias)


def solution(mesh):
    return jax.shard_map(
        per_device,
        mesh=mesh,
        in_specs=(
            P("lat", "lon", None),
            P("lat", "lon", None),
            P("lat", "lon", None),
            P("lat", "lon", None),
            P("lat"),
            P("lon"),
            P(),
        ),
        out_specs=(
            P("lat", "lon", None),
            P("lat", "lon", None),
            P("lat", "lon", None),
            P("lat", "lon", None),
            P(),
        ),
        check_vma=False,
    )
```

```python
import jax
import jax.numpy as jnp
from jax import lax
from jax.sharding import PartitionSpec as P


def padded_2(value, sides, width, wrap):
    for axis, dim in sides:
        size, length = (lax.axis_size(axis), value.shape[dim])
        up = [(i, (i + 1) % size) for i in range(size if wrap else size - 1)]
        down = [(j, i) for i, j in up]
        last = lax.slice_in_dim(value, length - width, length, axis=dim)
        leading = lax.slice_in_dim(value, 0, width, axis=dim)
        before = lax.ppermute(last, axis, up)
        after = lax.ppermute(leading, axis, down)
        value = jnp.concatenate([before, value, after], axis=dim)
    return value


def rims_of(array, along):
    if along == 0:
        return jnp.concatenate((array[:8], array[-8:]), axis=0)
    return jnp.concatenate((array[:, :8], array[:, -8:]), axis=1)


def settle(array, arrived, along):
    if along == 0:
        inner = array[8:-8]
        inner = inner.at[:8].add(arrived[:8])
        return inner.at[-8:].add(arrived[-8:])
    inner = array[:, 8:-8]
    inner = inner.at[:, :8].add(arrived[:, :8])
    return inner.at[:, -8:].add(arrived[:, -8:])


def exchange_sum(value, axis, flip):
    size = lax.axis_size(axis)
    pairs = [(i, i ^ flip) for i in range(size)]
    return value + lax.ppermute(value, axis, pairs)


def all_sum(value):
    for axis, flips in (("lon", (1, 2, 4, 8, 16, 48)), ("lat", (1, 3, 4, 12))):
        for flip in flips:
            value = exchange_sum(value, axis, flip)
    return value


def per_device(
    queries, key_vectors, value_vectors, out_cotangent, lat_start, lon_start, window_bias
):
    height, breadth, model_width = queries.shape
    head_count, window, _ = window_bias.shape
    head_dim = model_width // head_count
    score_scale = head_dim ** (-0.5)
    lon_total = breadth * lax.axis_size("lon")
    first_row = lax.axis_index("lat") * height
    first_col = lax.axis_index("lon") * breadth
    stacked = jnp.concatenate((key_vectors, value_vectors), axis=-1)
    tall = padded_2(stacked, (("lat", 0),), 8, False)
    padded = padded_2(tall, (("lon", 1),), 8, True)
    rows, cols = height + 16, breadth + 16
    cells, keys = height * breadth, rows * cols
    exact = lax.Precision.HIGHEST

    rel_rows = lat_start - (first_row - 8)
    rel_cols = (lon_start - (first_col - 8)) % lon_total
    places = jnp.arange(window, dtype=jnp.int32)
    key_index = jnp.arange(keys, dtype=jnp.int32)
    row_off = (key_index // cols)[None, :] - rel_rows[:, None]
    col_off = (key_index % cols)[None, :] - rel_cols[:, None]
    row_hot = (row_off[:, None, :] == places[None, :, None]).astype(jnp.float32)
    col_hot = (col_off[:, None, :] == places[None, :, None]).astype(jnp.float32)
    half_bias = jnp.sum(window_bias[:, None, :, :, None] * row_hot[None, :, :, None, :], axis=2)
    bias = jnp.sum(half_bias[:, :, None, :, :] * col_hot[None, None, :, :, :], axis=3)
    bias = bias.reshape(head_count, cells, keys)
    row_in = (row_off >= 0) & (row_off < window)
    col_in = (col_off >= 0) & (col_off < window)
    inside = (row_in[:, None, :] & col_in[None, :, :]).reshape(cells, keys)

    query_heads = queries.reshape(cells, head_count, head_dim)
    key_heads = padded[..., :model_width].reshape(keys, head_count, head_dim)
    value_heads = padded[..., model_width:].reshape(keys, head_count, head_dim)
    grad_heads = out_cotangent.reshape(cells, head_count, head_dim)
    scores = (
        jnp.einsum("qhd,khd->hqk", query_heads, key_heads, preferred_element_type=jnp.float32)
        * score_scale
        + bias
    )
    scores = jnp.where(inside[None], scores, -jnp.inf)
    row_peak = jnp.max(scores, axis=-1, keepdims=True)
    weights_raw = jnp.exp(scores - row_peak)
    row_total = jnp.sum(weights_raw, axis=-1, keepdims=True)
    attention = weights_raw / row_total
    rounded_probs = attention.astype(jnp.bfloat16)
    output = jnp.einsum(
        "hqk,khd->qhd", rounded_probs, value_heads, preferred_element_type=jnp.float32
    )
    attention_out = output.astype(jnp.bfloat16).reshape(height, breadth, model_width)
    dprobs = jnp.einsum("qhd,khd->hqk", grad_heads, value_heads, preferred_element_type=jnp.float32)
    correction = jnp.sum(attention * dprobs, axis=-1, keepdims=True)
    dscore = attention * (dprobs - correction)
    dscore_round = dscore.astype(jnp.bfloat16)
    grad_cells = dscore.reshape(head_count, height, breadth, keys)
    by_col = jnp.sum(grad_cells[:, :, :, None, :] * col_hot[None, None, :, :, :], axis=2)
    grad_table = jnp.einsum("hibk,iak->hab", by_col, row_hot, precision=exact)
    grad_window_bias = all_sum(grad_table)
    grad_table, dscore_round, rounded_probs = lax.optimization_barrier(
        (grad_table, dscore_round, rounded_probs)
    )
    grad_query = (
        jnp.einsum("hqk,khd->qhd", dscore_round, key_heads, preferred_element_type=jnp.float32)
        * score_scale
    )
    grad_queries = grad_query.astype(jnp.bfloat16).reshape(height, breadth, model_width)
    grad_keys = (
        jnp.einsum("hqk,qhd->khd", dscore_round, query_heads, preferred_element_type=jnp.float32)
        * score_scale
    )
    grad_vals = jnp.einsum(
        "hqk,qhd->khd", rounded_probs, grad_heads, preferred_element_type=jnp.float32
    )
    accum = jnp.concatenate(
        (grad_keys.reshape(rows, cols, model_width), grad_vals.reshape(rows, cols, model_width)),
        axis=-1,
    )
    arrived_cols = padded_2(rims_of(accum, 1).astype(jnp.bfloat16), (("lon", 1),), 8, True).astype(
        jnp.float32
    )
    folded = settle(accum, arrived_cols, 1)
    arrived = padded_2(rims_of(folded, 0).astype(jnp.bfloat16), (("lat", 0),), 8, False).astype(
        jnp.float32
    )
    totals = settle(folded, arrived, 0)
    grad_keys = totals[..., :model_width].astype(jnp.bfloat16)
    grad_values = totals[..., model_width:].astype(jnp.bfloat16)
    return (attention_out, grad_queries, grad_keys, grad_values, grad_window_bias)


def solution(mesh):
    return jax.shard_map(
        per_device,
        mesh=mesh,
        in_specs=(
            P("lat", "lon", None),
            P("lat", "lon", None),
            P("lat", "lon", None),
            P("lat", "lon", None),
            P("lat"),
            P("lon"),
            P(),
        ),
        out_specs=(
            P("lat", "lon", None),
            P("lat", "lon", None),
            P("lat", "lon", None),
            P("lat", "lon", None),
            P(),
        ),
        check_vma=False,
    )
```

```python
import jax
import jax.numpy as jnp
from jax import lax
from jax.sharding import PartitionSpec as P


def padded_2(value, sides, width, wrap):
    for axis, dim in sides:
        size, length = (lax.axis_size(axis), value.shape[dim])
        up = [(i, (i + 1) % size) for i in range(size if wrap else size - 1)]
        down = [(j, i) for i, j in up]
        last = lax.slice_in_dim(value, length - width, length, axis=dim)
        leading = lax.slice_in_dim(value, 0, width, axis=dim)
        before = lax.ppermute(last, axis, up)
        after = lax.ppermute(leading, axis, down)
        value = jnp.concatenate([before, value, after], axis=dim)
    return value


def rims_of(array, along):
    if along == 0:
        return jnp.concatenate((array[:8], array[-8:]), axis=0)
    return jnp.concatenate((array[:, :8], array[:, -8:]), axis=1)


def settle(array, arrived, along):
    if along == 0:
        inner = array[8:-8]
        inner = inner.at[:8].add(arrived[:8])
        return inner.at[-8:].add(arrived[-8:])
    inner = array[:, 8:-8]
    inner = inner.at[:, :8].add(arrived[:, :8])
    return inner.at[:, -8:].add(arrived[:, -8:])


def exchange_sum(value, axis, flip):
    size = lax.axis_size(axis)
    pairs = [(i, i ^ flip) for i in range(size)]
    return value + lax.ppermute(value, axis, pairs)


def all_sum(value):
    for axis, flips in (("lon", (1, 2, 4, 8, 16, 48)), ("lat", (1, 3, 4, 12))):
        for flip in flips:
            value = exchange_sum(value, axis, flip)
    return value


def per_device(
    queries, key_vectors, value_vectors, out_cotangent, lat_start, lon_start, window_bias
):
    height, breadth, model_width = queries.shape
    head_count, window, _ = window_bias.shape
    head_dim = model_width // head_count
    score_scale = head_dim ** (-0.5)
    lon_total = breadth * lax.axis_size("lon")
    first_row = lax.axis_index("lat") * height
    first_col = lax.axis_index("lon") * breadth
    stacked = jnp.concatenate((key_vectors, value_vectors), axis=-1)
    tall = padded_2(stacked, (("lat", 0),), 8, False)
    padded = padded_2(tall, (("lon", 1),), 8, True)
    rows, cols = height + 16, breadth + 16
    cells, keys = height * breadth, rows * cols
    exact = lax.Precision.HIGHEST

    rel_rows = lat_start - (first_row - 8)
    rel_cols = (lon_start - (first_col - 8)) % lon_total
    places = jnp.arange(window, dtype=jnp.int32)
    key_index = jnp.arange(keys, dtype=jnp.int32)
    row_off = (key_index // cols)[None, :] - rel_rows[:, None]
    col_off = (key_index % cols)[None, :] - rel_cols[:, None]
    row_hot = (row_off[:, None, :] == places[None, :, None]).astype(jnp.float32)
    col_hot = (col_off[:, None, :] == places[None, :, None]).astype(jnp.float32)
    half_bias = jnp.sum(window_bias[:, None, :, :, None] * row_hot[None, :, :, None, :], axis=2)
    bias = jnp.sum(half_bias[:, :, None, :, :] * col_hot[None, None, :, :, :], axis=3)
    bias = bias.reshape(head_count, cells, keys)
    row_in = (row_off >= 0) & (row_off < window)
    col_in = (col_off >= 0) & (col_off < window)
    inside = (row_in[:, None, :] & col_in[None, :, :]).reshape(cells, keys)

    query_heads = queries.reshape(cells, head_count, head_dim)
    key_heads = padded[..., :model_width].reshape(keys, head_count, head_dim)
    value_heads = padded[..., model_width:].reshape(keys, head_count, head_dim)
    grad_heads = out_cotangent.reshape(cells, head_count, head_dim)
    scores = (
        jnp.einsum("qhd,khd->hqk", query_heads, key_heads, preferred_element_type=jnp.float32)
        * score_scale
        + bias
    )
    scores = jnp.where(inside[None], scores, -jnp.inf)
    row_peak = jnp.max(scores, axis=-1, keepdims=True)
    weights_raw = jnp.exp(scores - row_peak)
    row_total = jnp.sum(weights_raw, axis=-1, keepdims=True)
    attention = weights_raw / row_total
    rounded_probs = attention.astype(jnp.bfloat16)
    output = jnp.einsum(
        "hqk,khd->qhd", rounded_probs, value_heads, preferred_element_type=jnp.float32
    )
    attention_out = output.astype(jnp.bfloat16).reshape(height, breadth, model_width)
    dprobs = jnp.einsum("qhd,khd->hqk", grad_heads, value_heads, preferred_element_type=jnp.float32)
    correction = jnp.sum(attention * dprobs, axis=-1, keepdims=True)
    dscore = attention * (dprobs - correction)
    dscore_round = dscore.astype(jnp.bfloat16)
    grad_query = (
        jnp.einsum("hqk,khd->qhd", dscore_round, key_heads, preferred_element_type=jnp.float32)
        * score_scale
    )
    grad_queries = grad_query.astype(jnp.bfloat16).reshape(height, breadth, model_width)
    grad_cells = dscore.reshape(head_count, height, breadth, keys)
    by_col = jnp.sum(grad_cells[:, :, :, None, :] * col_hot[None, None, :, :, :], axis=2)
    grad_table = jnp.einsum(
        "hibk,iak->hab", by_col, row_hot, precision=lax.Precision.HIGH
    )
    grad_keys = (
        jnp.einsum("hqk,qhd->khd", dscore_round, query_heads, preferred_element_type=jnp.float32)
        * score_scale
    )
    grad_vals = jnp.einsum(
        "hqk,qhd->khd", rounded_probs, grad_heads, preferred_element_type=jnp.float32
    )
    accum = jnp.concatenate(
        (grad_keys.reshape(rows, cols, model_width), grad_vals.reshape(rows, cols, model_width)),
        axis=-1,
    )
    arrived_cols = padded_2(rims_of(accum, 1).astype(jnp.bfloat16), (("lon", 1),), 8, True).astype(
        jnp.float32
    )
    folded = settle(accum, arrived_cols, 1)
    arrived = padded_2(rims_of(folded, 0).astype(jnp.bfloat16), (("lat", 0),), 8, False).astype(
        jnp.float32
    )
    totals = settle(folded, arrived, 0)
    grad_keys = totals[..., :model_width].astype(jnp.bfloat16)
    grad_values = totals[..., model_width:].astype(jnp.bfloat16)
    grad_window_bias = all_sum(grad_table)
    return (attention_out, grad_queries, grad_keys, grad_values, grad_window_bias)


def solution(mesh):
    return jax.shard_map(
        per_device,
        mesh=mesh,
        in_specs=(
            P("lat", "lon", None),
            P("lat", "lon", None),
            P("lat", "lon", None),
            P("lat", "lon", None),
            P("lat"),
            P("lon"),
            P(),
        ),
        out_specs=(
            P("lat", "lon", None),
            P("lat", "lon", None),
            P("lat", "lon", None),
            P("lat", "lon", None),
            P(),
        ),
        check_vma=False,
    )
```

```python
import jax
import jax.numpy as jnp
from jax import lax
from jax.sharding import PartitionSpec as P


def padded_2(value, sides, width, wrap):
    for axis, dim in sides:
        size, length = (lax.axis_size(axis), value.shape[dim])
        up = [(i, (i + 1) % size) for i in range(size if wrap else size - 1)]
        down = [(j, i) for i, j in up]
        last = lax.slice_in_dim(value, length - width, length, axis=dim)
        leading = lax.slice_in_dim(value, 0, width, axis=dim)
        before = lax.ppermute(last, axis, up)
        after = lax.ppermute(leading, axis, down)
        value = jnp.concatenate([before, value, after], axis=dim)
    return value


def rims_of(array, along):
    if along == 0:
        return jnp.concatenate((array[:8], array[-8:]), axis=0)
    return jnp.concatenate((array[:, :8], array[:, -8:]), axis=1)


def settle(array, arrived, along):
    if along == 0:
        inner = array[8:-8]
        inner = inner.at[:8].add(arrived[:8])
        return inner.at[-8:].add(arrived[-8:])
    inner = array[:, 8:-8]
    inner = inner.at[:, :8].add(arrived[:, :8])
    return inner.at[:, -8:].add(arrived[:, -8:])


def exchange_sum(value, axis, flip):
    size = lax.axis_size(axis)
    pairs = [(i, i ^ flip) for i in range(size)]
    return value + lax.ppermute(value, axis, pairs)


def all_sum(value):
    for axis, flips in (("lon", (1, 2, 4, 8, 16, 48)), ("lat", (1, 3, 4, 12))):
        for flip in flips:
            value = exchange_sum(value, axis, flip)
    return value


def per_device(
    queries, key_vectors, value_vectors, out_cotangent, lat_start, lon_start, window_bias
):
    height, breadth, model_width = queries.shape
    head_count, window, _ = window_bias.shape
    head_dim = model_width // head_count
    score_scale = head_dim ** (-0.5)
    lon_total = breadth * lax.axis_size("lon")
    first_row = lax.axis_index("lat") * height
    first_col = lax.axis_index("lon") * breadth
    stacked = jnp.concatenate((key_vectors, value_vectors), axis=-1)
    tall = padded_2(stacked, (("lat", 0),), 8, False)
    padded = padded_2(tall, (("lon", 1),), 8, True)
    rows, cols = height + 16, breadth + 16
    cells, keys = height * breadth, rows * cols
    exact = lax.Precision.HIGHEST

    rel_rows = lat_start - (first_row - 8)
    rel_cols = (lon_start - (first_col - 8)) % lon_total
    places = jnp.arange(window, dtype=jnp.int32)
    key_index = jnp.arange(keys, dtype=jnp.int32)
    row_off = (key_index // cols)[None, :] - rel_rows[:, None]
    col_off = (key_index % cols)[None, :] - rel_cols[:, None]
    row_hot = (row_off[:, None, :] == places[None, :, None]).astype(jnp.float32)
    col_hot = (col_off[:, None, :] == places[None, :, None]).astype(jnp.float32)
    half_bias = jnp.sum(window_bias[:, None, :, :, None] * row_hot[None, :, :, None, :], axis=2)
    bias = jnp.sum(half_bias[:, :, None, :, :] * col_hot[None, None, :, :, :], axis=3)
    bias = bias.reshape(head_count, cells, keys)
    row_in = (row_off >= 0) & (row_off < window)
    col_in = (col_off >= 0) & (col_off < window)
    inside = (row_in[:, None, :] & col_in[None, :, :]).reshape(cells, keys)

    query_heads = queries.reshape(cells, head_count, head_dim)
    key_heads = padded[..., :model_width].reshape(keys, head_count, head_dim)
    value_heads = padded[..., model_width:].reshape(keys, head_count, head_dim)
    grad_heads = out_cotangent.reshape(cells, head_count, head_dim)
    scores = (
        jnp.einsum("qhd,khd->hqk", query_heads, key_heads, preferred_element_type=jnp.float32)
        * score_scale
        + bias
    )
    scores = jnp.where(inside[None], scores, -jnp.inf)
    row_peak = jnp.max(scores, axis=-1, keepdims=True)
    weights_raw = jnp.exp(scores - row_peak)
    row_total = jnp.sum(weights_raw, axis=-1, keepdims=True)
    attention = weights_raw / row_total
    rounded_probs = attention.astype(jnp.bfloat16)
    output = jnp.einsum(
        "hqk,khd->qhd", rounded_probs, value_heads, preferred_element_type=jnp.float32
    )
    attention_out = output.astype(jnp.bfloat16).reshape(height, breadth, model_width)
    dprobs = jnp.einsum("qhd,khd->hqk", grad_heads, value_heads, preferred_element_type=jnp.float32)
    correction = jnp.sum(attention * dprobs, axis=-1, keepdims=True)
    dscore = attention * (dprobs - correction)
    dscore_round = dscore.astype(jnp.bfloat16)
    grad_query = (
        jnp.einsum("hqk,khd->qhd", dscore_round, key_heads, preferred_element_type=jnp.float32)
        * score_scale
    )
    grad_queries = grad_query.astype(jnp.bfloat16).reshape(height, breadth, model_width)
    grad_cells = dscore.reshape(head_count, height, breadth, keys)
    by_row = jnp.sum(grad_cells[:, :, None, :, :] * row_hot[None, :, :, None, :], axis=1)
    grad_table = jnp.einsum(
        "hajk,jbk->hab", by_row, col_hot, precision=lax.Precision.HIGH
    )
    grad_keys = (
        jnp.einsum("hqk,qhd->khd", dscore_round, query_heads, preferred_element_type=jnp.float32)
        * score_scale
    )
    grad_vals = jnp.einsum(
        "hqk,qhd->khd", rounded_probs, grad_heads, preferred_element_type=jnp.float32
    )
    accum = jnp.concatenate(
        (grad_keys.reshape(rows, cols, model_width), grad_vals.reshape(rows, cols, model_width)),
        axis=-1,
    )
    arrived_cols = padded_2(rims_of(accum, 1).astype(jnp.bfloat16), (("lon", 1),), 8, True).astype(
        jnp.float32
    )
    folded = settle(accum, arrived_cols, 1)
    arrived = padded_2(rims_of(folded, 0).astype(jnp.bfloat16), (("lat", 0),), 8, False).astype(
        jnp.float32
    )
    totals = settle(folded, arrived, 0)
    grad_keys = totals[..., :model_width].astype(jnp.bfloat16)
    grad_values = totals[..., model_width:].astype(jnp.bfloat16)
    grad_window_bias = all_sum(grad_table)
    return (attention_out, grad_queries, grad_keys, grad_values, grad_window_bias)


def solution(mesh):
    return jax.shard_map(
        per_device,
        mesh=mesh,
        in_specs=(
            P("lat", "lon", None),
            P("lat", "lon", None),
            P("lat", "lon", None),
            P("lat", "lon", None),
            P("lat"),
            P("lon"),
            P(),
        ),
        out_specs=(
            P("lat", "lon", None),
            P("lat", "lon", None),
            P("lat", "lon", None),
            P("lat", "lon", None),
            P(),
        ),
        check_vma=False,
    )
```

```python
import jax
import jax.numpy as jnp
from jax import lax
from jax.sharding import PartitionSpec as P


def padded_2(value, sides, width, wrap):
    for axis, dim in sides:
        size, length = (lax.axis_size(axis), value.shape[dim])
        up = [(i, (i + 1) % size) for i in range(size if wrap else size - 1)]
        down = [(j, i) for i, j in up]
        last = lax.slice_in_dim(value, length - width, length, axis=dim)
        leading = lax.slice_in_dim(value, 0, width, axis=dim)
        before = lax.ppermute(last, axis, up)
        after = lax.ppermute(leading, axis, down)
        value = jnp.concatenate([before, value, after], axis=dim)
    return value


def rims_of(array, along):
    if along == 0:
        return jnp.concatenate((array[:8], array[-8:]), axis=0)
    return jnp.concatenate((array[:, :8], array[:, -8:]), axis=1)


def settle(array, arrived, along):
    if along == 0:
        inner = array[8:-8]
        inner = inner.at[:8].add(arrived[:8])
        return inner.at[-8:].add(arrived[-8:])
    inner = array[:, 8:-8]
    inner = inner.at[:, :8].add(arrived[:, :8])
    return inner.at[:, -8:].add(arrived[:, -8:])


def exchange_sum(value, axis, flip):
    size = lax.axis_size(axis)
    pairs = [(i, i ^ flip) for i in range(size)]
    return value + lax.ppermute(value, axis, pairs)


def all_sum(value):
    for axis, flips in (("lon", (1, 2, 4, 8, 16, 48)), ("lat", (1, 3, 4, 12))):
        for flip in flips:
            value = exchange_sum(value, axis, flip)
    return value


def per_device(
    queries, key_vectors, value_vectors, out_cotangent, lat_start, lon_start, window_bias
):
    height, breadth, model_width = queries.shape
    head_count, window, _ = window_bias.shape
    head_dim = model_width // head_count
    score_scale = head_dim ** (-0.5)
    lon_total = breadth * lax.axis_size("lon")
    first_row = lax.axis_index("lat") * height
    first_col = lax.axis_index("lon") * breadth
    stacked = jnp.concatenate((key_vectors, value_vectors), axis=-1)
    tall = padded_2(stacked, (("lat", 0),), 8, False)
    padded = padded_2(tall, (("lon", 1),), 8, True)
    rows, cols = height + 16, breadth + 16
    cells, keys = height * breadth, rows * cols
    exact = lax.Precision.HIGHEST

    rel_rows = lat_start - (first_row - 8)
    rel_cols = (lon_start - (first_col - 8)) % lon_total
    places = jnp.arange(window, dtype=jnp.int32)
    key_index = jnp.arange(keys, dtype=jnp.int32)
    row_off = (key_index // cols)[None, :] - rel_rows[:, None]
    col_off = (key_index % cols)[None, :] - rel_cols[:, None]
    row_hot = (row_off[:, None, :] == places[None, :, None]).astype(jnp.float32)
    col_hot = (col_off[:, None, :] == places[None, :, None]).astype(jnp.float32)
    half_bias = jnp.sum(window_bias[:, None, :, :, None] * row_hot[None, :, :, None, :], axis=2)
    bias = jnp.sum(half_bias[:, :, None, :, :] * col_hot[None, None, :, :, :], axis=3)
    bias = bias.reshape(head_count, cells, keys)
    row_in = (row_off >= 0) & (row_off < window)
    col_in = (col_off >= 0) & (col_off < window)
    inside = (row_in[:, None, :] & col_in[None, :, :]).reshape(cells, keys)

    query_heads = queries.reshape(cells, head_count, head_dim)
    key_heads = padded[..., :model_width].reshape(keys, head_count, head_dim)
    value_heads = padded[..., model_width:].reshape(keys, head_count, head_dim)
    grad_heads = out_cotangent.reshape(cells, head_count, head_dim)
    scores = (
        jnp.einsum("qhd,khd->hqk", query_heads, key_heads, preferred_element_type=jnp.float32)
        * score_scale
        + bias
    )
    scores = jnp.where(inside[None], scores, -jnp.inf)
    row_peak = jnp.max(scores, axis=-1, keepdims=True)
    weights_raw = jnp.exp(scores - row_peak)
    row_total = jnp.sum(weights_raw, axis=-1, keepdims=True)
    attention = weights_raw / row_total
    rounded_probs = attention.astype(jnp.bfloat16)
    output = jnp.einsum(
        "hqk,khd->qhd", rounded_probs, value_heads, preferred_element_type=jnp.float32
    )
    attention_out = output.astype(jnp.bfloat16).reshape(height, breadth, model_width)
    dprobs = jnp.einsum("qhd,khd->hqk", grad_heads, value_heads, preferred_element_type=jnp.float32)
    correction = jnp.sum(attention * dprobs, axis=-1, keepdims=True)
    dscore = attention * (dprobs - correction)
    dscore_round = dscore.astype(jnp.bfloat16)
    grad_query = (
        jnp.einsum("hqk,khd->qhd", dscore_round, key_heads, preferred_element_type=jnp.float32)
        * score_scale
    )
    grad_queries = grad_query.astype(jnp.bfloat16).reshape(height, breadth, model_width)
    grad_cells = dscore.reshape(head_count, height, breadth, keys)
    by_row = jnp.sum(grad_cells[:, :, None, :, :] * row_hot[None, :, :, None, :], axis=1)
    grad_table = jnp.einsum(
        "hajk,jbk->hab", by_row, col_hot, precision=lax.Precision.HIGH
    )
    own_head = jnp.arange(head_count, dtype=jnp.int32)[:, None, None] == (
        jnp.arange(model_width, dtype=jnp.int32) // head_dim
    )[None, None, :]
    query_blocks = jnp.where(own_head, queries.reshape(1, cells, model_width), 0)
    grad_blocks = jnp.where(own_head, out_cotangent.reshape(1, cells, model_width), 0)
    grad_keys = (
        jnp.einsum(
            "pk,pf->kf",
            dscore_round.reshape(head_count * cells, keys),
            query_blocks.reshape(head_count * cells, model_width),
            preferred_element_type=jnp.float32,
        )
        * score_scale
    )
    grad_vals = jnp.einsum(
        "pk,pf->kf",
        rounded_probs.reshape(head_count * cells, keys),
        grad_blocks.reshape(head_count * cells, model_width),
        preferred_element_type=jnp.float32,
    )
    accum = jnp.concatenate(
        (grad_keys.reshape(rows, cols, model_width), grad_vals.reshape(rows, cols, model_width)),
        axis=-1,
    )
    arrived_cols = padded_2(rims_of(accum, 1).astype(jnp.bfloat16), (("lon", 1),), 8, True).astype(
        jnp.float32
    )
    folded = settle(accum, arrived_cols, 1)
    arrived = padded_2(rims_of(folded, 0).astype(jnp.bfloat16), (("lat", 0),), 8, False).astype(
        jnp.float32
    )
    totals = settle(folded, arrived, 0)
    grad_keys = totals[..., :model_width].astype(jnp.bfloat16)
    grad_values = totals[..., model_width:].astype(jnp.bfloat16)
    grad_window_bias = all_sum(grad_table)
    return (attention_out, grad_queries, grad_keys, grad_values, grad_window_bias)


def solution(mesh):
    return jax.shard_map(
        per_device,
        mesh=mesh,
        in_specs=(
            P("lat", "lon", None),
            P("lat", "lon", None),
            P("lat", "lon", None),
            P("lat", "lon", None),
            P("lat"),
            P("lon"),
            P(),
        ),
        out_specs=(
            P("lat", "lon", None),
            P("lat", "lon", None),
            P("lat", "lon", None),
            P("lat", "lon", None),
            P(),
        ),
        check_vma=False,
    )
```
